512 devices in a mesh: island: 64 (over z, x, y_hi), fsdp: 8 (over y_lo, core).
Axes of the slice: x: 4, y: 8 (y_hi: 2, y_lo: 4; y = y_hi * 4 + y_lo), z: 8, core: 2. Of those that a mesh axis runs over, the one named last changes fastest.
Arguments:
- hidden: bfloat16 [64, 1024, 8192], P('island', 'fsdp'), may hold values from -6 to 6
- gain: bfloat16 [8192], P('fsdp'), may hold values from 0.5 to 1.5
- doc_ids: int32 [64, 1024], P('island', 'fsdp'), may hold values from 0 to 7, never falling along the last dimension, each value on 1 to 256 neighbouring positions
- cotangent: bfloat16 [64, 1024, 512], P('island', 'fsdp'), may hold values from -0.1796875 to 0.1796875
- pseudo_grad: bfloat16 [64, 8192, 512], P('island', 'fsdp'), may hold values from -0.75 to 0.75
- outer_weight: float32 [8192, 512], P(('fsdp', 'island')), may hold values from -0.0625 to 0.0625
- momentum: float32 [8192, 512], P(('fsdp', 'island')), may hold values from -0.0625 to 0.0625
Outputs:
- keys: bfloat16 [64, 1024, 512], P('island', 'fsdp')
- grad_weight: bfloat16 [64, 8192, 512], P('island', 'fsdp')
- grad_gain: float32 [64, 8192], P('island', 'fsdp')
- new_outer: float32 [8192, 512], P(('fsdp', 'island'))
- new_momentum: float32 [8192, 512], P(('fsdp', 'island'))
The draws below stay inside these ranges and needn't reach their ends.
Inputs may be any that keep to these rules, and one draw needn't show every extreme that they name: `doc_ids`: document numbers never fall along a replica's sequence; every document holds 1 to 256 tokens, and one holds exactly 256.
All inputs are finite; a program needn't handle non-finite values.
Results may differ from the reference program's by a relative error of at most 0.014.
Values may be sent and summed in bfloat16 or wider, within the bound.
No kernel may reach another device: no remote copies, remote signals or barrier semaphores. Data moves between devices by JAX's collectives and lax.ppermute only.
A program may use at most 128 MiB of HBM per device.

```python
import math
import jax
import jax.numpy as jnp
import numpy as np
from jax import lax

D = 8192
HEAD = 128
TOK_DEV = 128
DOCS = 8
COLS = 512
SEQ = 1024
ISLANDS = 64
N_ISLAND = 64
N_FSDP = 8


def spiked(drawn, rng, source, target, shards_of, factor):
    owner, partner = [(jnp.arange(drawn.shape[dim]) // (drawn.shape[dim] // shards_of)).reshape([-1 if axis == dim else 1 for axis in range(drawn.ndim)]) for dim in (source, target)]
    chosen = jax.random.permutation(rng, shards_of)[partner]
    strong = (owner == chosen) | (owner == (partner + shards_of // 2) % shards_of)
    return jnp.where(strong, factor * drawn, drawn)


def level_of(stream_key, shape, shards, smallest, largest):
    factor_of = 1.0
    for dim, parts in shards:
        heights = jax.random.uniform(jax.random.fold_in(jax.random.fold_in(stream_key, 6), dim), (parts,), jnp.float32, smallest / len(shards), largest / len(shards))
        factor_of = factor_of * jnp.repeat(jnp.exp(heights), shape[dim] // parts).reshape((-1,) + (1,) * (len(shape) - 1 - dim))
    return factor_of


def split_up(amount, total, limit, lean):
    weights = [(1 << 20) // math.isqrt(grade ** lean) + 1 for grade in range(2, amount + 1)]
    surplus, counts = total - limit - (amount - 1), [1] * (amount - 1)
    while surplus > 0:
        movable = [i for i in range(amount - 1) if counts[i] < limit]
        mass, remaining = sum([weights[i] for i in movable]), surplus
        for i in movable:
            extra = min(limit - counts[i], max(1, remaining * weights[i] // mass), surplus)
            counts[i] = counts[i] + extra
            surplus = surplus - extra
    return np.array([limit] + counts)


def ragged(stream_key, count, total, limit, slope):
    if count == 2:
        one = jax.random.randint(stream_key, (), max(1, total - limit), min(limit, total - 1) + 1)
        return jnp.stack([one, total - one])
    lengths = jnp.asarray(split_up(count, total, limit, slope), jnp.int32)
    twos = (count - 1) // 2
    donor, sink = lengths[1:1 + 2 * twos:2], lengths[2:2 + 2 * twos:2]
    slack = jnp.minimum(donor - 1, limit - sink)
    shifted = jax.random.randint(jax.random.fold_in(stream_key, 1), (twos,), 0, 1 << 20) % (slack + 1)
    lengths = lengths.at[1:1 + 2 * twos:2].set(donor - shifted).at[2:2 + 2 * twos:2].set(sink + shifted)
    return lengths[jax.random.permutation(jax.random.fold_in(stream_key, 2), count)]


def normal_values(key, extent, scale, limit, pieces=(), kind=jnp.bfloat16):
    result = scale * jax.random.normal(key, extent, jnp.float32)
    if pieces:
        result = result * level_of(key, extent, pieces, -0.22, 0.18)
    return jnp.clip(result, -limit, limit).astype(kind)


def bell_draw_with(own_key, dims, deviation, most, pieces, heavy, kind=jnp.bfloat16):
    array = deviation * jax.random.normal(own_key, dims, jnp.float32)
    if pieces:
        array = array * level_of(own_key, dims, pieces, -0.22, 0.18)
    return jnp.clip(spiked(array, jax.random.fold_in(own_key, 3), *heavy), -most, most).astype(kind)


def setup_inputs(seed: int = 0) -> dict:
    arg_keys = jax.random.split(jax.random.key(seed), 8)
    return {
        "hidden": normal_values(arg_keys[0], (ISLANDS, SEQ, D), 1.0, 6.0, ((0, 64), (1, 8))),
        "gain": jnp.clip(1.0 + 0.1 * jax.random.normal(arg_keys[1], (D,), jnp.float32), 0.5, 1.5).astype(jnp.bfloat16),
        "doc_ids": jax.vmap(lambda own: jnp.searchsorted(jnp.cumsum(ragged(own, DOCS, SEQ, SEQ // 4, 1)), jnp.arange(SEQ), side="right"))(jax.random.split(arg_keys[2], ISLANDS)).reshape((ISLANDS, SEQ)).astype(jnp.int32),
        "cotangent": normal_values(arg_keys[3], (ISLANDS, SEQ, COLS), 0.03, 0.1796875, ((0, 64), (1, 8))),
        "pseudo_grad": bell_draw_with(arg_keys[4], (ISLANDS, D, COLS), (D // 16) ** -0.5, 0.75, ((0, 64), (1, 8)), (0, 1, 64, 4.0)),
        "outer_weight": normal_values(arg_keys[5], (D, COLS), D ** -0.5, 0.0625, ((0, 512),), jnp.float32),
        "momentum": normal_values(arg_keys[6], (D, COLS), D ** -0.5, 0.0625, ((0, 512),), jnp.float32),
    }


learn_rate = 0.7
momentum_rate = 0.9
norm_eps = 1e-05
rope_base = 500000.0
far_index = 1 << 30

def angles_for(positions, head_width):
    half_width = head_width // 2
    frequency = jnp.exp(jnp.arange(half_width, dtype=jnp.float32) * (-2.0 * math.log(rope_base) / head_width))
    phases = positions[:, None] * frequency[None, :]
    return (jnp.cos(phases), jnp.sin(phases))

def rotate(values, cosine, sine_part, sign):
    rows = values.shape[0]
    half_width = cosine.shape[1]
    shaped = values.reshape(rows, -1, 2 * half_width)
    leading = shaped[:, :, :half_width]
    second = shaped[:, :, half_width:]
    cos_b = cosine[:, None, :]
    sin_b = sine_part[:, None, :] * sign
    joined = jnp.concatenate([leading * cos_b - second * sin_b, second * cos_b + leading * sin_b], axis=2)
    return joined.reshape(rows, -1)

def reference(hidden, gain, doc_ids, cotangent, pseudo_grad, outer_weight, momentum):
    mean_delta = lax.optimization_barrier(jnp.sum(pseudo_grad.astype(jnp.float32), axis=0)) / N_ISLAND
    new_momentum = momentum_rate * momentum + mean_delta
    new_outer = outer_weight - learn_rate * (mean_delta + momentum_rate * new_momentum)
    weight = new_outer.astype(jnp.bfloat16)
    gain_f = gain.astype(jnp.float32)

    def replica(items):
        states, doc_row, cot_row = items
        seq_len = states.shape[0]
        indices = jnp.arange(seq_len, dtype=jnp.int32)
        documents = jnp.arange(DOCS, dtype=jnp.int32)
        in_document = doc_row[:, None] == documents[None, :]
        starts = lax.optimization_barrier(jnp.min(jnp.where(in_document, indices[:, None], far_index), axis=0))
        doc_start = lax.optimization_barrier(jnp.sum(jnp.where(in_document, starts[None, :], 0), axis=1))
        positions = (indices - doc_start).astype(jnp.float32)
        cosine, sine_part = angles_for(positions, HEAD)
        hidden_f = states.astype(jnp.float32)
        row_scale = lax.rsqrt(lax.optimization_barrier(jnp.mean(hidden_f * hidden_f, axis=1, keepdims=True)) + norm_eps)
        normed = hidden_f * row_scale
        activations = (normed * gain_f[None, :]).astype(jnp.bfloat16)
        projected = jnp.dot(activations, weight, preferred_element_type=jnp.float32)
        rotated = rotate(projected, cosine, sine_part, 1.0).astype(jnp.bfloat16)
        back_grad = rotate(cot_row.astype(jnp.float32), cosine, sine_part, -1.0).astype(jnp.bfloat16)
        hidden_grad = jnp.dot(back_grad, weight.T, preferred_element_type=jnp.float32)
        grad_gain = lax.optimization_barrier(jnp.sum(hidden_grad * normed, axis=0))
        act_blocks = activations.reshape(N_FSDP, TOK_DEV, D).astype(jnp.float32)
        back_blocks = back_grad.reshape(N_FSDP, TOK_DEV, COLS).astype(jnp.float32)
        block_parts = jnp.einsum('btd,bth->bdh', act_blocks, back_blocks).astype(jnp.bfloat16)
        grad_weight = lax.optimization_barrier(jnp.sum(block_parts.astype(jnp.float32), axis=0)).astype(jnp.bfloat16)
        return (rotated, grad_weight, grad_gain)
    keys, grad_weight, grad_gain = lax.map(replica, (hidden, doc_ids, cotangent))
    return (keys, grad_weight, grad_gain, new_outer, new_momentum)
```

```python
import math

import jax
import jax.numpy as jnp
import numpy as np
from jax import lax
from jax.sharding import Mesh
from jax.sharding import PartitionSpec as P

HEAD = 128
DOCS = 8


learn_rate = 0.7
momentum_rate = 0.9
norm_eps = 1e-05
rope_base = 500000.0
far_index = 1 << 30

ISLAND_FACTORS = None


def angles_for(positions, head_width):
    half_width = head_width // 2
    frequency = jnp.exp(
        jnp.arange(half_width, dtype=jnp.float32) * (-2.0 * math.log(rope_base) / head_width)
    )
    phases = positions[:, None] * frequency[None, :]
    return (jnp.cos(phases), jnp.sin(phases))


def rotate(values, cosine, sine_part, sign):
    rows = values.shape[0]
    half_width = cosine.shape[1]
    shaped = values.reshape(rows, -1, 2 * half_width)
    leading = shaped[:, :, :half_width]
    second = shaped[:, :, half_width:]
    cos_b = cosine[:, None, :]
    sin_b = sine_part[:, None, :] * sign
    joined = jnp.concatenate(
        [leading * cos_b - second * sin_b, second * cos_b + leading * sin_b], axis=2
    )
    return joined.reshape(rows, -1)


def body(island_axes, hidden, gain, doc_ids, cotangent, pseudo_grad, outer_weight, momentum):
    islands = 1
    for ax in island_axes:
        islands *= lax.axis_size(ax)
    fsdp_ways = lax.axis_size("fsdp")

    summed = pseudo_grad[0].astype(jnp.float32)
    for ax in island_axes:
        summed = lax.psum_scatter(summed, ax, scatter_dimension=0, tiled=True)
    mean_delta = summed / islands
    new_momentum = momentum_rate * momentum + mean_delta
    new_outer = outer_weight - learn_rate * (mean_delta + momentum_rate * new_momentum)
    weight_shard = new_outer.astype(jnp.bfloat16)
    for ax in reversed(island_axes):
        weight_shard = lax.all_gather(weight_shard, ax, axis=0, tiled=True)

    tok_rows = hidden.shape[1]
    seq = tok_rows * fsdp_ways
    me = lax.axis_index("fsdp")
    all_docs = lax.all_gather(doc_ids[0], "fsdp", axis=0, tiled=True)
    indices = jnp.arange(seq, dtype=jnp.int32)
    documents = jnp.arange(DOCS, dtype=jnp.int32)
    in_document = all_docs[:, None] == documents[None, :]
    starts = jnp.min(jnp.where(in_document, indices[:, None], far_index), axis=0)
    doc_start = jnp.sum(jnp.where(in_document, starts[None, :], 0), axis=1)
    positions = (indices - doc_start).astype(jnp.float32)
    cosine, sine_part = angles_for(positions, HEAD)
    all_cot = lax.all_gather(cotangent[0], "fsdp", axis=0, tiled=True)
    all_back = rotate(all_cot.astype(jnp.float32), cosine, sine_part, -1.0).astype(jnp.bfloat16)

    hidden_f = hidden[0].astype(jnp.float32)
    row_scale = lax.rsqrt(jnp.mean(hidden_f * hidden_f, axis=1, keepdims=True) + norm_eps)
    all_scales = lax.all_gather(row_scale, "fsdp", axis=0, tiled=True)
    columns = lax.all_to_all(hidden[0], "fsdp", split_axis=1, concat_axis=0, tiled=True)
    normed_cols = columns.astype(jnp.float32) * all_scales
    act_cols = (normed_cols * gain.astype(jnp.float32)[None, :]).astype(jnp.bfloat16)

    grad_weight = jnp.zeros((act_cols.shape[1], all_back.shape[1]), jnp.float32)
    for block in range(fsdp_ways):
        act_block = act_cols[block * tok_rows : (block + 1) * tok_rows]
        back_block = all_back[block * tok_rows : (block + 1) * tok_rows]
        part = lax.dot_general(
            act_block, back_block, (((0,), (0,)), ((), ())), preferred_element_type=jnp.float32
        )
        grad_weight = grad_weight + part.astype(jnp.bfloat16).astype(jnp.float32)

    hidden_grad = lax.dot_general(
        all_back, weight_shard, (((1,), (1,)), ((), ())), preferred_element_type=jnp.float32
    )
    grad_gain = jnp.sum(hidden_grad * normed_cols, axis=0)

    partial_keys = jnp.dot(act_cols, weight_shard, preferred_element_type=jnp.float32)
    projected = lax.psum_scatter(partial_keys, "fsdp", scatter_dimension=0, tiled=True)
    my_cos = lax.dynamic_slice_in_dim(cosine, me * tok_rows, tok_rows, axis=0)
    my_sin = lax.dynamic_slice_in_dim(sine_part, me * tok_rows, tok_rows, axis=0)
    rotated = rotate(projected, my_cos, my_sin, 1.0).astype(jnp.bfloat16)
    return (
        rotated[None],
        grad_weight.astype(jnp.bfloat16)[None],
        grad_gain[None],
        new_outer,
        new_momentum,
    )


def _island_factors(n):
    if ISLAND_FACTORS is not None:
        return tuple(ISLAND_FACTORS)
    if n == 64:
        return (8, 4, 2)
    return (n,)


def solution(mesh):
    factors = _island_factors(mesh.shape["island"])
    island_axes = tuple(f"island{k}" for k in range(len(factors)))
    devices = np.asarray(mesh.devices).reshape(factors + (mesh.shape["fsdp"],))
    fine = Mesh(devices, island_axes + ("fsdp",))
    isl = island_axes
    placed = (
        P(isl, "fsdp", None),
        P("fsdp"),
        P(isl, "fsdp"),
        P(isl, "fsdp", None),
        P(isl, "fsdp", None),
        P(("fsdp",) + isl, None),
        P(("fsdp",) + isl, None),
    )
    return jax.shard_map(
        lambda *a: body(island_axes, *a),
        mesh=fine,
        in_specs=placed,
        out_specs=(
            P(isl, "fsdp", None),
            P(isl, "fsdp", None),
            P(isl, "fsdp"),
            P(("fsdp",) + isl, None),
            P(("fsdp",) + isl, None),
        ),
        check_vma=False,
    )
```

```python
import math

import jax
import jax.numpy as jnp
import numpy as np
from jax import lax
from jax.sharding import Mesh
from jax.sharding import PartitionSpec as P

HEAD = 128
DOCS = 8


learn_rate = 0.7
momentum_rate = 0.9
norm_eps = 1e-05
rope_base = 500000.0
far_index = 1 << 30

ISLAND_FACTORS = None


def angles_for(positions, head_width):
    half_width = head_width // 2
    frequency = jnp.exp(
        jnp.arange(half_width, dtype=jnp.float32) * (-2.0 * math.log(rope_base) / head_width)
    )
    phases = positions[:, None] * frequency[None, :]
    return (jnp.cos(phases), jnp.sin(phases))


def rotate(values, cosine, sine_part, sign):
    rows = values.shape[0]
    half_width = cosine.shape[1]
    shaped = values.reshape(rows, -1, 2 * half_width)
    leading = shaped[:, :, :half_width]
    second = shaped[:, :, half_width:]
    cos_b = cosine[:, None, :]
    sin_b = sine_part[:, None, :] * sign
    joined = jnp.concatenate(
        [leading * cos_b - second * sin_b, second * cos_b + leading * sin_b], axis=2
    )
    return joined.reshape(rows, -1)


def body(island_axes, hidden, gain, doc_ids, cotangent, pseudo_grad, outer_weight, momentum):
    islands = 1
    for ax in island_axes:
        islands *= lax.axis_size(ax)
    fsdp_ways = lax.axis_size("fsdp")

    stages = (island_axes[:1], island_axes[1:]) if len(island_axes) > 1 else (island_axes,)
    summed = pseudo_grad[0].astype(jnp.float32)
    for axes in stages:
        summed = lax.psum_scatter(summed, axes, scatter_dimension=0, tiled=True)
    mean_delta = summed / islands
    new_momentum = momentum_rate * momentum + mean_delta
    new_outer = outer_weight - learn_rate * (mean_delta + momentum_rate * new_momentum)
    weight_shard = new_outer.astype(jnp.bfloat16)
    for axes in reversed(stages):
        weight_shard = lax.all_gather(weight_shard, axes, axis=0, tiled=True)

    tok_rows = hidden.shape[1]
    seq = tok_rows * fsdp_ways
    me = lax.axis_index("fsdp")
    all_docs = lax.all_gather(doc_ids[0], "fsdp", axis=0, tiled=True)
    indices = jnp.arange(seq, dtype=jnp.int32)
    documents = jnp.arange(DOCS, dtype=jnp.int32)
    in_document = all_docs[:, None] == documents[None, :]
    starts = jnp.min(jnp.where(in_document, indices[:, None], far_index), axis=0)
    doc_start = jnp.sum(jnp.where(in_document, starts[None, :], 0), axis=1)
    positions = (indices - doc_start).astype(jnp.float32)
    cosine, sine_part = angles_for(positions, HEAD)
    width = hidden.shape[2] // fsdp_ways
    cols_out = cotangent.shape[2]
    outgoing = jnp.concatenate(
        [
            hidden[0].reshape(tok_rows, fsdp_ways, width).transpose(1, 0, 2),
            jnp.broadcast_to(cotangent[0][None], (fsdp_ways, tok_rows, cols_out)),
        ],
        axis=2,
    )
    incoming = lax.all_to_all(outgoing, "fsdp", split_axis=0, concat_axis=0, tiled=True)
    columns = incoming[:, :, :width].reshape(seq, width)
    all_cot = incoming[:, :, width:].reshape(seq, cols_out)
    all_back = rotate(all_cot.astype(jnp.float32), cosine, sine_part, -1.0).astype(jnp.bfloat16)

    hidden_f = hidden[0].astype(jnp.float32)
    row_scale = lax.rsqrt(jnp.mean(hidden_f * hidden_f, axis=1, keepdims=True) + norm_eps)
    all_scales = lax.all_gather(row_scale, "fsdp", axis=0, tiled=True)
    normed_cols = columns.astype(jnp.float32) * all_scales
    act_cols = (normed_cols * gain.astype(jnp.float32)[None, :]).astype(jnp.bfloat16)

    grad_weight = jnp.zeros((act_cols.shape[1], all_back.shape[1]), jnp.float32)
    for block in range(fsdp_ways):
        act_block = act_cols[block * tok_rows : (block + 1) * tok_rows]
        back_block = all_back[block * tok_rows : (block + 1) * tok_rows]
        part = lax.dot_general(
            act_block, back_block, (((0,), (0,)), ((), ())), preferred_element_type=jnp.float32
        )
        grad_weight = grad_weight + part.astype(jnp.bfloat16).astype(jnp.float32)

    hidden_grad = lax.dot_general(
        all_back, weight_shard, (((1,), (1,)), ((), ())), preferred_element_type=jnp.float32
    )
    grad_gain = jnp.sum(hidden_grad * normed_cols, axis=0)

    partial_keys = jnp.dot(act_cols, weight_shard, preferred_element_type=jnp.float32)
    projected = lax.psum_scatter(partial_keys, "fsdp", scatter_dimension=0, tiled=True)
    my_cos = lax.dynamic_slice_in_dim(cosine, me * tok_rows, tok_rows, axis=0)
    my_sin = lax.dynamic_slice_in_dim(sine_part, me * tok_rows, tok_rows, axis=0)
    rotated = rotate(projected, my_cos, my_sin, 1.0).astype(jnp.bfloat16)
    return (
        rotated[None],
        grad_weight.astype(jnp.bfloat16)[None],
        grad_gain[None],
        new_outer,
        new_momentum,
    )


def _island_factors(n):
    if ISLAND_FACTORS is not None:
        return tuple(ISLAND_FACTORS)
    if n == 64:
        return (8, 4, 2)
    return (n,)


def solution(mesh):
    factors = _island_factors(mesh.shape["island"])
    island_axes = tuple(f"island{k}" for k in range(len(factors)))
    devices = np.asarray(mesh.devices).reshape(factors + (mesh.shape["fsdp"],))
    fine = Mesh(devices, island_axes + ("fsdp",))
    isl = island_axes
    placed = (
        P(isl, "fsdp", None),
        P("fsdp"),
        P(isl, "fsdp"),
        P(isl, "fsdp", None),
        P(isl, "fsdp", None),
        P(("fsdp",) + isl, None),
        P(("fsdp",) + isl, None),
    )
    return jax.shard_map(
        lambda *a: body(island_axes, *a),
        mesh=fine,
        in_specs=placed,
        out_specs=(
            P(isl, "fsdp", None),
            P(isl, "fsdp", None),
            P(isl, "fsdp"),
            P(("fsdp",) + isl, None),
            P(("fsdp",) + isl, None),
        ),
        check_vma=False,
    )
```

```python
import math

import jax
import jax.numpy as jnp
import numpy as np
from jax import lax
from jax.sharding import Mesh
from jax.sharding import PartitionSpec as P

HEAD = 128
DOCS = 8


learn_rate = 0.7
momentum_rate = 0.9
norm_eps = 1e-05
rope_base = 500000.0
far_index = 1 << 30

ISLAND_FACTORS = None


def angles_for(positions, head_width):
    half_width = head_width // 2
    frequency = jnp.exp(
        jnp.arange(half_width, dtype=jnp.float32) * (-2.0 * math.log(rope_base) / head_width)
    )
    phases = positions[:, None] * frequency[None, :]
    return (jnp.cos(phases), jnp.sin(phases))


def rotate(values, cosine, sine_part, sign):
    rows = values.shape[0]
    half_width = cosine.shape[1]
    shaped = values.reshape(rows, -1, 2 * half_width)
    leading = shaped[:, :, :half_width]
    second = shaped[:, :, half_width:]
    cos_b = cosine[:, None, :]
    sin_b = sine_part[:, None, :] * sign
    joined = jnp.concatenate(
        [leading * cos_b - second * sin_b, second * cos_b + leading * sin_b], axis=2
    )
    return joined.reshape(rows, -1)


def halving_scatter(values, axis):
    n = lax.axis_size(axis)
    me = lax.axis_index(axis)
    step = n // 2
    while step >= 1:
        rows = values.shape[0] // 2
        upper = (me // step) % 2
        keep = lax.dynamic_slice_in_dim(values, upper * rows, rows, axis=0)
        send = lax.dynamic_slice_in_dim(values, (1 - upper) * rows, rows, axis=0)
        got = lax.ppermute(send, axis, [(j, j ^ step) for j in range(n)])
        values = keep + got
        step //= 2
    return values


def doubling_gather(values, axis):
    n = lax.axis_size(axis)
    me = lax.axis_index(axis)
    step = 1
    while step < n:
        got = lax.ppermute(values, axis, [(j, j ^ step) for j in range(n)])
        upper = (me // step) % 2
        values = jnp.where(
            upper == 1,
            jnp.concatenate([got, values], axis=0),
            jnp.concatenate([values, got], axis=0),
        )
        step *= 2
    return values


def body(island_axes, hidden, gain, doc_ids, cotangent, pseudo_grad, outer_weight, momentum):
    islands = 1
    for ax in island_axes:
        islands *= lax.axis_size(ax)
    fsdp_ways = lax.axis_size("fsdp")

    summed = pseudo_grad[0].astype(jnp.float32)
    summed = lax.psum_scatter(summed, island_axes[0], scatter_dimension=0, tiled=True)
    for ax in island_axes[1:]:
        summed = halving_scatter(summed, ax)
    mean_delta = summed / islands
    new_momentum = momentum_rate * momentum + mean_delta
    new_outer = outer_weight - learn_rate * (mean_delta + momentum_rate * new_momentum)
    weight_shard = new_outer.astype(jnp.bfloat16)
    for ax in reversed(island_axes[1:]):
        weight_shard = doubling_gather(weight_shard, ax)
    weight_shard = lax.all_gather(weight_shard, island_axes[0], axis=0, tiled=True)

    tok_rows = hidden.shape[1]
    seq = tok_rows * fsdp_ways
    me = lax.axis_index("fsdp")
    all_docs = lax.all_gather(doc_ids[0], "fsdp", axis=0, tiled=True)
    indices = jnp.arange(seq, dtype=jnp.int32)
    documents = jnp.arange(DOCS, dtype=jnp.int32)
    in_document = all_docs[:, None] == documents[None, :]
    starts = jnp.min(jnp.where(in_document, indices[:, None], far_index), axis=0)
    doc_start = jnp.sum(jnp.where(in_document, starts[None, :], 0), axis=1)
    positions = (indices - doc_start).astype(jnp.float32)
    cosine, sine_part = angles_for(positions, HEAD)
    width = hidden.shape[2] // fsdp_ways
    cols_out = cotangent.shape[2]
    outgoing = jnp.concatenate(
        [
            hidden[0].reshape(tok_rows, fsdp_ways, width).transpose(1, 0, 2),
            jnp.broadcast_to(cotangent[0][None], (fsdp_ways, tok_rows, cols_out)),
        ],
        axis=2,
    )
    incoming = lax.all_to_all(outgoing, "fsdp", split_axis=0, concat_axis=0, tiled=True)
    columns = incoming[:, :, :width].reshape(seq, width)
    all_cot = incoming[:, :, width:].reshape(seq, cols_out)
    all_back = rotate(all_cot.astype(jnp.float32), cosine, sine_part, -1.0).astype(jnp.bfloat16)

    hidden_f = hidden[0].astype(jnp.float32)
    row_scale = lax.rsqrt(jnp.mean(hidden_f * hidden_f, axis=1, keepdims=True) + norm_eps)
    all_scales = lax.all_gather(row_scale, "fsdp", axis=0, tiled=True)
    normed_cols = columns.astype(jnp.float32) * all_scales
    act_cols = (normed_cols * gain.astype(jnp.float32)[None, :]).astype(jnp.bfloat16)

    grad_weight = jnp.zeros((act_cols.shape[1], all_back.shape[1]), jnp.float32)
    for block in range(fsdp_ways):
        act_block = act_cols[block * tok_rows : (block + 1) * tok_rows]
        back_block = all_back[block * tok_rows : (block + 1) * tok_rows]
        part = lax.dot_general(
            act_block, back_block, (((0,), (0,)), ((), ())), preferred_element_type=jnp.float32
        )
        grad_weight = grad_weight + part.astype(jnp.bfloat16).astype(jnp.float32)

    hidden_grad = lax.dot_general(
        all_back, weight_shard, (((1,), (1,)), ((), ())), preferred_element_type=jnp.float32
    )
    grad_gain = jnp.sum(hidden_grad * normed_cols, axis=0)

    partial_keys = jnp.dot(act_cols, weight_shard, preferred_element_type=jnp.float32)
    projected = lax.psum_scatter(partial_keys, "fsdp", scatter_dimension=0, tiled=True)
    my_cos = lax.dynamic_slice_in_dim(cosine, me * tok_rows, tok_rows, axis=0)
    my_sin = lax.dynamic_slice_in_dim(sine_part, me * tok_rows, tok_rows, axis=0)
    rotated = rotate(projected, my_cos, my_sin, 1.0).astype(jnp.bfloat16)
    return (
        rotated[None],
        grad_weight.astype(jnp.bfloat16)[None],
        grad_gain[None],
        new_outer,
        new_momentum,
    )


def _island_factors(n):
    if ISLAND_FACTORS is not None:
        return tuple(ISLAND_FACTORS)
    if n == 64:
        return (8, 4, 2)
    return (n,)


def solution(mesh):
    factors = _island_factors(mesh.shape["island"])
    island_axes = tuple(f"island{k}" for k in range(len(factors)))
    devices = np.asarray(mesh.devices).reshape(factors + (mesh.shape["fsdp"],))
    fine = Mesh(devices, island_axes + ("fsdp",))
    isl = island_axes
    placed = (
        P(isl, "fsdp", None),
        P("fsdp"),
        P(isl, "fsdp"),
        P(isl, "fsdp", None),
        P(isl, "fsdp", None),
        P(("fsdp",) + isl, None),
        P(("fsdp",) + isl, None),
    )
    return jax.shard_map(
        lambda *a: body(island_axes, *a),
        mesh=fine,
        in_specs=placed,
        out_specs=(
            P(isl, "fsdp", None),
            P(isl, "fsdp", None),
            P(isl, "fsdp"),
            P(("fsdp",) + isl, None),
            P(("fsdp",) + isl, None),
        ),
        check_vma=False,
    )
```

```python
import math

import jax
import jax.numpy as jnp
import numpy as np
from jax import lax
from jax.sharding import Mesh
from jax.sharding import PartitionSpec as P

HEAD = 128
DOCS = 8


learn_rate = 0.7
momentum_rate = 0.9
norm_eps = 1e-05
rope_base = 500000.0
far_index = 1 << 30

ISLAND_FACTORS = None


def angles_for(positions, head_width):
    half_width = head_width // 2
    frequency = jnp.exp(
        jnp.arange(half_width, dtype=jnp.float32) * (-2.0 * math.log(rope_base) / head_width)
    )
    phases = positions[:, None] * frequency[None, :]
    return (jnp.cos(phases), jnp.sin(phases))


def rotate(values, cosine, sine_part, sign):
    rows = values.shape[0]
    half_width = cosine.shape[1]
    shaped = values.reshape(rows, -1, 2 * half_width)
    leading = shaped[:, :, :half_width]
    second = shaped[:, :, half_width:]
    cos_b = cosine[:, None, :]
    sin_b = sine_part[:, None, :] * sign
    joined = jnp.concatenate(
        [leading * cos_b - second * sin_b, second * cos_b + leading * sin_b], axis=2
    )
    return joined.reshape(rows, -1)


def group_index(axes):
    me = 0
    for ax in axes:
        me = me * lax.axis_size(ax) + lax.axis_index(ax)
    return me


def exchange_scatter(values, axes):
    n = 1
    for ax in axes:
        n *= lax.axis_size(ax)
    me = group_index(axes)
    blocks = values.reshape((n, values.shape[0] // n) + values.shape[1:])
    total = lax.dynamic_index_in_dim(blocks, me, axis=0, keepdims=False).astype(jnp.float32)
    for d in range(1, n):
        send = lax.dynamic_index_in_dim(blocks, me ^ d, axis=0, keepdims=False)
        got = lax.ppermute(send, axes, [(j, j ^ d) for j in range(n)])
        total = total + got.astype(jnp.float32)
    return total


def exchange_gather(values, axes):
    n = 1
    for ax in axes:
        n *= lax.axis_size(ax)
    me = group_index(axes)
    arrived = [values] + [
        lax.ppermute(values, axes, [(j, j ^ d) for j in range(n)]) for d in range(1, n)
    ]
    stacked = jnp.stack(arrived)
    ordered = jnp.take(stacked, me ^ jnp.arange(n, dtype=me.dtype), axis=0)
    return ordered.reshape((n * values.shape[0],) + values.shape[1:])


def body(island_axes, hidden, gain, doc_ids, cotangent, pseudo_grad, outer_weight, momentum):
    islands = 1
    for ax in island_axes:
        islands *= lax.axis_size(ax)
    fsdp_ways = lax.axis_size("fsdp")

    summed = exchange_scatter(pseudo_grad[0], island_axes[:1])
    if len(island_axes) > 1:
        summed = exchange_scatter(summed, island_axes[1:])
    mean_delta = summed / islands
    new_momentum = momentum_rate * momentum + mean_delta
    new_outer = outer_weight - learn_rate * (mean_delta + momentum_rate * new_momentum)
    weight_shard = new_outer.astype(jnp.bfloat16)
    if len(island_axes) > 1:
        weight_shard = exchange_gather(weight_shard, island_axes[1:])
    weight_shard = exchange_gather(weight_shard, island_axes[:1])

    tok_rows = hidden.shape[1]
    seq = tok_rows * fsdp_ways
    me = lax.axis_index("fsdp")
    indices = jnp.arange(seq, dtype=jnp.int32)
    documents = jnp.arange(DOCS, dtype=jnp.int32)
    hidden_f = hidden[0].astype(jnp.float32)
    row_scale = lax.rsqrt(jnp.mean(hidden_f * hidden_f, axis=1, keepdims=True) + norm_eps)
    width = hidden.shape[2] // fsdp_ways
    cols_out = cotangent.shape[2]
    scale_high = lax.reduce_precision(row_scale, exponent_bits=8, mantissa_bits=7)
    scale_mid = lax.reduce_precision(row_scale - scale_high, exponent_bits=8, mantissa_bits=7)
    scale_low = row_scale - scale_high - scale_mid
    extras = jnp.concatenate(
        [doc_ids[0][:, None].astype(jnp.float32), scale_high, scale_mid, scale_low], axis=1
    ).astype(jnp.bfloat16)
    extras = jnp.pad(extras, ((0, 0), (0, 128 - extras.shape[1])))
    outgoing = jnp.concatenate(
        [
            hidden[0].reshape(tok_rows, fsdp_ways, width).transpose(1, 0, 2),
            jnp.broadcast_to(cotangent[0][None], (fsdp_ways, tok_rows, cols_out)),
            jnp.broadcast_to(extras[None], (fsdp_ways,) + extras.shape),
        ],
        axis=2,
    )
    incoming = lax.all_to_all(outgoing, "fsdp", split_axis=0, concat_axis=0, tiled=True)
    columns = incoming[:, :, :width].reshape(seq, width)
    all_cot = incoming[:, :, width : width + cols_out].reshape(seq, cols_out)
    all_extras = incoming[:, :, width + cols_out :].reshape(seq, -1).astype(jnp.float32)
    all_docs = all_extras[:, 0].astype(jnp.int32)
    all_scales = (all_extras[:, 1:2] + all_extras[:, 2:3]) + all_extras[:, 3:4]
    in_document = all_docs[:, None] == documents[None, :]
    starts = jnp.min(jnp.where(in_document, indices[:, None], far_index), axis=0)
    doc_start = jnp.sum(jnp.where(in_document, starts[None, :], 0), axis=1)
    positions = (indices - doc_start).astype(jnp.float32)
    cosine, sine_part = angles_for(positions, HEAD)
    all_back = rotate(all_cot.astype(jnp.float32), cosine, sine_part, -1.0).astype(jnp.bfloat16)

    normed_cols = columns.astype(jnp.float32) * all_scales
    act_cols = (normed_cols * gain.astype(jnp.float32)[None, :]).astype(jnp.bfloat16)

    grad_weight = jnp.zeros((act_cols.shape[1], all_back.shape[1]), jnp.float32)
    for block in range(fsdp_ways):
        act_block = act_cols[block * tok_rows : (block + 1) * tok_rows]
        back_block = all_back[block * tok_rows : (block + 1) * tok_rows]
        part = lax.dot_general(
            act_block, back_block, (((0,), (0,)), ((), ())), preferred_element_type=jnp.float32
        )
        grad_weight = grad_weight + part.astype(jnp.bfloat16).astype(jnp.float32)

    hidden_grad = lax.dot_general(
        all_back, weight_shard, (((1,), (1,)), ((), ())), preferred_element_type=jnp.float32
    )
    grad_gain = jnp.sum(hidden_grad * normed_cols, axis=0)

    partial_keys = jnp.dot(act_cols, weight_shard, preferred_element_type=jnp.float32)
    projected = lax.psum_scatter(partial_keys, "fsdp", scatter_dimension=0, tiled=True)
    my_cos = lax.dynamic_slice_in_dim(cosine, me * tok_rows, tok_rows, axis=0)
    my_sin = lax.dynamic_slice_in_dim(sine_part, me * tok_rows, tok_rows, axis=0)
    rotated = rotate(projected, my_cos, my_sin, 1.0).astype(jnp.bfloat16)
    return (
        rotated[None],
        grad_weight.astype(jnp.bfloat16)[None],
        grad_gain[None],
        new_outer,
        new_momentum,
    )


def _island_factors(n):
    if ISLAND_FACTORS is not None:
        return tuple(ISLAND_FACTORS)
    if n == 64:
        return (8, 4, 2)
    return (n,)


def solution(mesh):
    factors = _island_factors(mesh.shape["island"])
    island_axes = tuple(f"island{k}" for k in range(len(factors)))
    devices = np.asarray(mesh.devices).reshape(factors + (mesh.shape["fsdp"],))
    fine = Mesh(devices, island_axes + ("fsdp",))
    isl = island_axes
    placed = (
        P(isl, "fsdp", None),
        P("fsdp"),
        P(isl, "fsdp"),
        P(isl, "fsdp", None),
        P(isl, "fsdp", None),
        P(("fsdp",) + isl, None),
        P(("fsdp",) + isl, None),
    )
    return jax.shard_map(
        lambda *a: body(island_axes, *a),
        mesh=fine,
        in_specs=placed,
        out_specs=(
            P(isl, "fsdp", None),
            P(isl, "fsdp", None),
            P(isl, "fsdp"),
            P(("fsdp",) + isl, None),
            P(("fsdp",) + isl, None),
        ),
        check_vma=False,
    )
```

```python
import math

import jax
import jax.numpy as jnp
import numpy as np
from jax import lax
from jax.sharding import Mesh
from jax.sharding import PartitionSpec as P

HEAD = 128
DOCS = 8


learn_rate = 0.7
momentum_rate = 0.9
norm_eps = 1e-05
rope_base = 500000.0
far_index = 1 << 30

ISLAND_FACTORS = None


def angles_for(positions, head_width):
    half_width = head_width // 2
    frequency = jnp.exp(
        jnp.arange(half_width, dtype=jnp.float32) * (-2.0 * math.log(rope_base) / head_width)
    )
    phases = positions[:, None] * frequency[None, :]
    return (jnp.cos(phases), jnp.sin(phases))


def rotate(values, cosine, sine_part, sign):
    rows = values.shape[0]
    half_width = cosine.shape[1]
    shaped = values.reshape(rows, -1, 2 * half_width)
    leading = shaped[:, :, :half_width]
    second = shaped[:, :, half_width:]
    cos_b = cosine[:, None, :]
    sin_b = sine_part[:, None, :] * sign
    joined = jnp.concatenate(
        [leading * cos_b - second * sin_b, second * cos_b + leading * sin_b], axis=2
    )
    return joined.reshape(rows, -1)


def group_size(axes):
    n = 1
    for ax in axes:
        n *= lax.axis_size(ax)
    return n


def exchange_scatter(values, axes):
    n = group_size(axes)
    blocks = values.reshape((n, values.shape[0] // n) + values.shape[1:])
    arrived = lax.all_to_all(blocks, axes, split_axis=0, concat_axis=0, tiled=True)
    return jnp.sum(arrived.astype(jnp.float32), axis=0)


def exchange_gather(values, axes):
    n = group_size(axes)
    repeated = jnp.broadcast_to(values[None], (n,) + values.shape)
    arrived = lax.all_to_all(repeated, axes, split_axis=0, concat_axis=0, tiled=True)
    return arrived.reshape((n * values.shape[0],) + values.shape[1:])


def body(island_axes, hidden, gain, doc_ids, cotangent, pseudo_grad, outer_weight, momentum):
    islands = 1
    for ax in island_axes:
        islands *= lax.axis_size(ax)
    fsdp_ways = lax.axis_size("fsdp")

    summed = exchange_scatter(pseudo_grad[0], island_axes[:1])
    if len(island_axes) > 1:
        summed = exchange_scatter(summed, island_axes[1:])
    mean_delta = summed / islands
    new_momentum = momentum_rate * momentum + mean_delta
    new_outer = outer_weight - learn_rate * (mean_delta + momentum_rate * new_momentum)
    weight_shard = new_outer.astype(jnp.bfloat16)
    if len(island_axes) > 1:
        weight_shard = exchange_gather(weight_shard, island_axes[1:])
    weight_shard = exchange_gather(weight_shard, island_axes[:1])

    tok_rows = hidden.shape[1]
    seq = tok_rows * fsdp_ways
    me = lax.axis_index("fsdp")
    indices = jnp.arange(seq, dtype=jnp.int32)
    documents = jnp.arange(DOCS, dtype=jnp.int32)
    hidden_f = hidden[0].astype(jnp.float32)
    row_scale = lax.rsqrt(jnp.mean(hidden_f * hidden_f, axis=1, keepdims=True) + norm_eps)
    width = hidden.shape[2] // fsdp_ways
    cols_out = cotangent.shape[2]
    scale_high = lax.reduce_precision(row_scale, exponent_bits=8, mantissa_bits=7)
    scale_mid = lax.reduce_precision(row_scale - scale_high, exponent_bits=8, mantissa_bits=7)
    scale_low = row_scale - scale_high - scale_mid
    extras = jnp.concatenate(
        [doc_ids[0][:, None].astype(jnp.float32), scale_high, scale_mid, scale_low], axis=1
    ).astype(jnp.bfloat16)
    extras = jnp.pad(extras, ((0, 0), (0, 128 - extras.shape[1])))
    outgoing = jnp.concatenate(
        [
            hidden[0].reshape(tok_rows, fsdp_ways, width).transpose(1, 0, 2),
            jnp.broadcast_to(cotangent[0][None], (fsdp_ways, tok_rows, cols_out)),
            jnp.broadcast_to(extras[None], (fsdp_ways,) + extras.shape),
        ],
        axis=2,
    )
    incoming = lax.all_to_all(outgoing, "fsdp", split_axis=0, concat_axis=0, tiled=True)
    columns = incoming[:, :, :width].reshape(seq, width)
    all_cot = incoming[:, :, width : width + cols_out].reshape(seq, cols_out)
    all_extras = incoming[:, :, width + cols_out :].reshape(seq, -1).astype(jnp.float32)
    all_docs = all_extras[:, 0].astype(jnp.int32)
    all_scales = (all_extras[:, 1:2] + all_extras[:, 2:3]) + all_extras[:, 3:4]
    in_document = all_docs[:, None] == documents[None, :]
    starts = jnp.min(jnp.where(in_document, indices[:, None], far_index), axis=0)
    doc_start = jnp.sum(jnp.where(in_document, starts[None, :], 0), axis=1)
    positions = (indices - doc_start).astype(jnp.float32)
    cosine, sine_part = angles_for(positions, HEAD)
    all_back = rotate(all_cot.astype(jnp.float32), cosine, sine_part, -1.0).astype(jnp.bfloat16)

    normed_cols = columns.astype(jnp.float32) * all_scales
    act_cols = (normed_cols * gain.astype(jnp.float32)[None, :]).astype(jnp.bfloat16)

    grad_weight = jnp.zeros((act_cols.shape[1], all_back.shape[1]), jnp.float32)
    for block in range(fsdp_ways):
        act_block = act_cols[block * tok_rows : (block + 1) * tok_rows]
        back_block = all_back[block * tok_rows : (block + 1) * tok_rows]
        part = lax.dot_general(
            act_block, back_block, (((0,), (0,)), ((), ())), preferred_element_type=jnp.float32
        )
        grad_weight = grad_weight + part.astype(jnp.bfloat16).astype(jnp.float32)

    hidden_grad = lax.dot_general(
        all_back, weight_shard, (((1,), (1,)), ((), ())), preferred_element_type=jnp.float32
    )
    grad_gain = jnp.sum(hidden_grad * normed_cols, axis=0)

    partial_keys = jnp.dot(act_cols, weight_shard, preferred_element_type=jnp.float32)
    projected = lax.psum_scatter(partial_keys, "fsdp", scatter_dimension=0, tiled=True)
    my_cos = lax.dynamic_slice_in_dim(cosine, me * tok_rows, tok_rows, axis=0)
    my_sin = lax.dynamic_slice_in_dim(sine_part, me * tok_rows, tok_rows, axis=0)
    rotated = rotate(projected, my_cos, my_sin, 1.0).astype(jnp.bfloat16)
    return (
        rotated[None],
        grad_weight.astype(jnp.bfloat16)[None],
        grad_gain[None],
        new_outer,
        new_momentum,
    )


def _island_factors(n):
    if ISLAND_FACTORS is not None:
        return tuple(ISLAND_FACTORS)
    if n == 64:
        return (8, 4, 2)
    return (n,)


def solution(mesh):
    factors = _island_factors(mesh.shape["island"])
    island_axes = tuple(f"island{k}" for k in range(len(factors)))
    devices = np.asarray(mesh.devices).reshape(factors + (mesh.shape["fsdp"],))
    fine = Mesh(devices, island_axes + ("fsdp",))
    isl = island_axes
    placed = (
        P(isl, "fsdp", None),
        P("fsdp"),
        P(isl, "fsdp"),
        P(isl, "fsdp", None),
        P(isl, "fsdp", None),
        P(("fsdp",) + isl, None),
        P(("fsdp",) + isl, None),
    )
    return jax.shard_map(
        lambda *a: body(island_axes, *a),
        mesh=fine,
        in_specs=placed,
        out_specs=(
            P(isl, "fsdp", None),
            P(isl, "fsdp", None),
            P(isl, "fsdp"),
            P(("fsdp",) + isl, None),
            P(("fsdp",) + isl, None),
        ),
        check_vma=False,
    )
```

```python
import math

import jax
import jax.numpy as jnp
import numpy as np
from jax import lax
from jax.sharding import Mesh
from jax.sharding import PartitionSpec as P

HEAD = 128
DOCS = 8


learn_rate = 0.7
momentum_rate = 0.9
norm_eps = 1e-05
rope_base = 500000.0
far_index = 1 << 30

ISLAND_FACTORS = None


def angles_for(positions, head_width):
    half_width = head_width // 2
    frequency = jnp.exp(
        jnp.arange(half_width, dtype=jnp.float32) * (-2.0 * math.log(rope_base) / head_width)
    )
    phases = positions[:, None] * frequency[None, :]
    return (jnp.cos(phases), jnp.sin(phases))


def rotate(values, cosine, sine_part, sign):
    rows = values.shape[0]
    half_width = cosine.shape[1]
    shaped = values.reshape(rows, -1, 2 * half_width)
    leading = shaped[:, :, :half_width]
    second = shaped[:, :, half_width:]
    cos_b = cosine[:, None, :]
    sin_b = sine_part[:, None, :] * sign
    joined = jnp.concatenate(
        [leading * cos_b - second * sin_b, second * cos_b + leading * sin_b], axis=2
    )
    return joined.reshape(rows, -1)


def halving_scatter(values, axis):
    n = lax.axis_size(axis)
    me = lax.axis_index(axis)
    step = n // 2
    while step >= 1:
        rows = values.shape[0] // 2
        upper = (me // step) % 2
        keep = lax.dynamic_slice_in_dim(values, upper * rows, rows, axis=0)
        send = lax.dynamic_slice_in_dim(values, (1 - upper) * rows, rows, axis=0)
        got = lax.ppermute(send, axis, [(j, j ^ step) for j in range(n)])
        values = keep + got
        step //= 2
    return values


def doubling_gather(values, axis):
    n = lax.axis_size(axis)
    me = lax.axis_index(axis)
    step = 1
    while step < n:
        got = lax.ppermute(values, axis, [(j, j ^ step) for j in range(n)])
        upper = (me // step) % 2
        values = jnp.where(
            upper == 1,
            jnp.concatenate([got, values], axis=0),
            jnp.concatenate([values, got], axis=0),
        )
        step *= 2
    return values


def gather_by_all_to_all(values, axis):
    n = lax.axis_size(axis)
    repeated = jnp.broadcast_to(values[None], (n,) + values.shape)
    arrived = lax.all_to_all(repeated, axis, split_axis=0, concat_axis=0, tiled=True)
    return arrived.reshape((n * values.shape[0],) + values.shape[1:])


def body(island_axes, hidden, gain, doc_ids, cotangent, pseudo_grad, outer_weight, momentum):
    islands = 1
    for ax in island_axes:
        islands *= lax.axis_size(ax)
    fsdp_ways = lax.axis_size("fsdp")

    summed = pseudo_grad[0].astype(jnp.float32)
    summed = lax.psum_scatter(summed, island_axes[0], scatter_dimension=0, tiled=True)
    for ax in island_axes[1:]:
        summed = halving_scatter(summed, ax)
    mean_delta = summed / islands
    new_momentum = momentum_rate * momentum + mean_delta
    new_outer = outer_weight - learn_rate * (mean_delta + momentum_rate * new_momentum)
    weight_shard = new_outer.astype(jnp.bfloat16)
    for ax in reversed(island_axes[1:]):
        weight_shard = doubling_gather(weight_shard, ax)
    weight_shard = gather_by_all_to_all(weight_shard, island_axes[0])

    tok_rows = hidden.shape[1]
    seq = tok_rows * fsdp_ways
    me = lax.axis_index("fsdp")
    indices = jnp.arange(seq, dtype=jnp.int32)
    documents = jnp.arange(DOCS, dtype=jnp.int32)
    hidden_f = hidden[0].astype(jnp.float32)
    row_scale = lax.rsqrt(jnp.mean(hidden_f * hidden_f, axis=1, keepdims=True) + norm_eps)
    width = hidden.shape[2] // fsdp_ways
    cols_out = cotangent.shape[2]
    scale_high = lax.reduce_precision(row_scale, exponent_bits=8, mantissa_bits=7)
    scale_mid = lax.reduce_precision(row_scale - scale_high, exponent_bits=8, mantissa_bits=7)
    scale_low = row_scale - scale_high - scale_mid
    extras = jnp.concatenate(
        [doc_ids[0][:, None].astype(jnp.float32), scale_high, scale_mid, scale_low], axis=1
    ).astype(jnp.bfloat16)
    extras = jnp.pad(extras, ((0, 0), (0, 128 - extras.shape[1])))
    outgoing = jnp.concatenate(
        [
            hidden[0].reshape(tok_rows, fsdp_ways, width).transpose(1, 0, 2),
            jnp.broadcast_to(cotangent[0][None], (fsdp_ways, tok_rows, cols_out)),
            jnp.broadcast_to(extras[None], (fsdp_ways,) + extras.shape),
        ],
        axis=2,
    )
    incoming = lax.all_to_all(outgoing, "fsdp", split_axis=0, concat_axis=0, tiled=True)
    columns = incoming[:, :, :width].reshape(seq, width)
    all_cot = incoming[:, :, width : width + cols_out].reshape(seq, cols_out)
    all_extras = incoming[:, :, width + cols_out :].reshape(seq, -1).astype(jnp.float32)
    all_docs = all_extras[:, 0].astype(jnp.int32)
    all_scales = (all_extras[:, 1:2] + all_extras[:, 2:3]) + all_extras[:, 3:4]
    in_document = all_docs[:, None] == documents[None, :]
    starts = jnp.min(jnp.where(in_document, indices[:, None], far_index), axis=0)
    doc_start = jnp.sum(jnp.where(in_document, starts[None, :], 0), axis=1)
    positions = (indices - doc_start).astype(jnp.float32)
    cosine, sine_part = angles_for(positions, HEAD)
    all_back = rotate(all_cot.astype(jnp.float32), cosine, sine_part, -1.0).astype(jnp.bfloat16)

    normed_cols = columns.astype(jnp.float32) * all_scales
    act_cols = (normed_cols * gain.astype(jnp.float32)[None, :]).astype(jnp.bfloat16)

    grad_weight = jnp.zeros((act_cols.shape[1], all_back.shape[1]), jnp.float32)
    for block in range(fsdp_ways):
        act_block = act_cols[block * tok_rows : (block + 1) * tok_rows]
        back_block = all_back[block * tok_rows : (block + 1) * tok_rows]
        part = lax.dot_general(
            act_block, back_block, (((0,), (0,)), ((), ())), preferred_element_type=jnp.float32
        )
        grad_weight = grad_weight + part.astype(jnp.bfloat16).astype(jnp.float32)

    hidden_grad = lax.dot_general(
        all_back, weight_shard, (((1,), (1,)), ((), ())), preferred_element_type=jnp.float32
    )
    grad_gain = jnp.sum(hidden_grad * normed_cols, axis=0)

    partial_keys = jnp.dot(act_cols, weight_shard, preferred_element_type=jnp.float32)
    projected = lax.psum_scatter(
        partial_keys.astype(jnp.bfloat16), "fsdp", scatter_dimension=0, tiled=True
    ).astype(jnp.float32)
    my_cos = lax.dynamic_slice_in_dim(cosine, me * tok_rows, tok_rows, axis=0)
    my_sin = lax.dynamic_slice_in_dim(sine_part, me * tok_rows, tok_rows, axis=0)
    rotated = rotate(projected, my_cos, my_sin, 1.0).astype(jnp.bfloat16)
    return (
        rotated[None],
        grad_weight.astype(jnp.bfloat16)[None],
        grad_gain[None],
        new_outer,
        new_momentum,
    )


def _island_factors(n):
    if ISLAND_FACTORS is not None:
        return tuple(ISLAND_FACTORS)
    if n == 64:
        return (8, 4, 2)
    return (n,)


def solution(mesh):
    factors = _island_factors(mesh.shape["island"])
    island_axes = tuple(f"island{k}" for k in range(len(factors)))
    devices = np.asarray(mesh.devices).reshape(factors + (mesh.shape["fsdp"],))
    fine = Mesh(devices, island_axes + ("fsdp",))
    isl = island_axes
    placed = (
        P(isl, "fsdp", None),
        P("fsdp"),
        P(isl, "fsdp"),
        P(isl, "fsdp", None),
        P(isl, "fsdp", None),
        P(("fsdp",) + isl, None),
        P(("fsdp",) + isl, None),
    )
    return jax.shard_map(
        lambda *a: body(island_axes, *a),
        mesh=fine,
        in_specs=placed,
        out_specs=(
            P(isl, "fsdp", None),
            P(isl, "fsdp", None),
            P(isl, "fsdp"),
            P(("fsdp",) + isl, None),
            P(("fsdp",) + isl, None),
        ),
        check_vma=False,
    )
```

```python
import math

import jax
import jax.numpy as jnp
import numpy as np
from jax import lax
from jax.sharding import Mesh
from jax.sharding import PartitionSpec as P

HEAD = 128
DOCS = 8


learn_rate = 0.7
momentum_rate = 0.9
norm_eps = 1e-05
rope_base = 500000.0
far_index = 1 << 30

ISLAND_FACTORS = None


def angles_for(positions, head_width):
    half_width = head_width // 2
    frequency = jnp.exp(
        jnp.arange(half_width, dtype=jnp.float32) * (-2.0 * math.log(rope_base) / head_width)
    )
    phases = positions[:, None] * frequency[None, :]
    return (jnp.cos(phases), jnp.sin(phases))


def rotate(values, cosine, sine_part, sign):
    rows = values.shape[0]
    half_width = cosine.shape[1]
    shaped = values.reshape(rows, -1, 2 * half_width)
    leading = shaped[:, :, :half_width]
    second = shaped[:, :, half_width:]
    cos_b = cosine[:, None, :]
    sin_b = sine_part[:, None, :] * sign
    joined = jnp.concatenate(
        [leading * cos_b - second * sin_b, second * cos_b + leading * sin_b], axis=2
    )
    return joined.reshape(rows, -1)


def halving_scatter(values, axis):
    n = lax.axis_size(axis)
    me = lax.axis_index(axis)
    step = n // 2
    while step >= 1:
        rows = values.shape[0] // 2
        upper = (me // step) % 2
        keep = lax.dynamic_slice_in_dim(values, upper * rows, rows, axis=0)
        send = lax.dynamic_slice_in_dim(values, (1 - upper) * rows, rows, axis=0)
        got = lax.ppermute(send, axis, [(j, j ^ step) for j in range(n)])
        values = keep + got
        step //= 2
    return values


def doubling_gather(values, axis):
    n = lax.axis_size(axis)
    me = lax.axis_index(axis)
    step = 1
    while step < n:
        got = lax.ppermute(values, axis, [(j, j ^ step) for j in range(n)])
        upper = (me // step) % 2
        values = jnp.where(
            upper == 1,
            jnp.concatenate([got, values], axis=0),
            jnp.concatenate([values, got], axis=0),
        )
        step *= 2
    return values


def scatter_by_all_to_all(values, axis):
    n = lax.axis_size(axis)
    blocks = values.reshape((n, values.shape[0] // n) + values.shape[1:])
    arrived = lax.all_to_all(blocks, axis, split_axis=0, concat_axis=0, tiled=True)
    return jnp.sum(arrived.astype(jnp.float32), axis=0)


def body(island_axes, hidden, gain, doc_ids, cotangent, pseudo_grad, outer_weight, momentum):
    islands = 1
    for ax in island_axes:
        islands *= lax.axis_size(ax)
    fsdp_ways = lax.axis_size("fsdp")

    first_stage = scatter_by_all_to_all(pseudo_grad[0], island_axes[0])
    summed = first_stage
    for ax in island_axes[1:]:
        summed = halving_scatter(summed, ax)
    mean_delta = summed / islands
    new_momentum = momentum_rate * momentum + mean_delta
    new_outer = outer_weight - learn_rate * (mean_delta + momentum_rate * new_momentum)
    weight_shard = new_outer.astype(jnp.bfloat16)
    for ax in reversed(island_axes[1:]):
        weight_shard = doubling_gather(weight_shard, ax)
    weight_shard = lax.all_gather(weight_shard, island_axes[0], axis=0, tiled=True)

    tok_rows = hidden.shape[1]
    seq = tok_rows * fsdp_ways
    me = lax.axis_index("fsdp")
    indices = jnp.arange(seq, dtype=jnp.int32)
    documents = jnp.arange(DOCS, dtype=jnp.int32)
    hidden_f = hidden[0].astype(jnp.float32)
    row_scale = lax.rsqrt(jnp.mean(hidden_f * hidden_f, axis=1, keepdims=True) + norm_eps)
    width = hidden.shape[2] // fsdp_ways
    cols_out = cotangent.shape[2]
    scale_high = lax.reduce_precision(row_scale, exponent_bits=8, mantissa_bits=7)
    scale_mid = lax.reduce_precision(row_scale - scale_high, exponent_bits=8, mantissa_bits=7)
    scale_low = row_scale - scale_high - scale_mid
    extras = jnp.concatenate(
        [doc_ids[0][:, None].astype(jnp.float32), scale_high, scale_mid, scale_low], axis=1
    ).astype(jnp.bfloat16)
    extras = jnp.pad(extras, ((0, 0), (0, 128 - extras.shape[1])))
    outgoing = jnp.concatenate(
        [
            hidden[0].reshape(tok_rows, fsdp_ways, width).transpose(1, 0, 2),
            jnp.broadcast_to(cotangent[0][None], (fsdp_ways, tok_rows, cols_out)),
            jnp.broadcast_to(extras[None], (fsdp_ways,) + extras.shape),
        ],
        axis=2,
    )
    _, outgoing = lax.optimization_barrier((first_stage, outgoing))
    incoming = lax.all_to_all(outgoing, "fsdp", split_axis=0, concat_axis=0, tiled=True)
    columns = incoming[:, :, :width].reshape(seq, width)
    all_cot = incoming[:, :, width : width + cols_out].reshape(seq, cols_out)
    all_extras = incoming[:, :, width + cols_out :].reshape(seq, -1).astype(jnp.float32)
    all_docs = all_extras[:, 0].astype(jnp.int32)
    all_scales = (all_extras[:, 1:2] + all_extras[:, 2:3]) + all_extras[:, 3:4]
    in_document = all_docs[:, None] == documents[None, :]
    starts = jnp.min(jnp.where(in_document, indices[:, None], far_index), axis=0)
    doc_start = jnp.sum(jnp.where(in_document, starts[None, :], 0), axis=1)
    positions = (indices - doc_start).astype(jnp.float32)
    cosine, sine_part = angles_for(positions, HEAD)
    all_back = rotate(all_cot.astype(jnp.float32), cosine, sine_part, -1.0).astype(jnp.bfloat16)

    normed_cols = columns.astype(jnp.float32) * all_scales
    act_cols = (normed_cols * gain.astype(jnp.float32)[None, :]).astype(jnp.bfloat16)

    grad_weight = jnp.zeros((act_cols.shape[1], all_back.shape[1]), jnp.float32)
    for block in range(fsdp_ways):
        act_block = act_cols[block * tok_rows : (block + 1) * tok_rows]
        back_block = all_back[block * tok_rows : (block + 1) * tok_rows]
        part = lax.dot_general(
            act_block, back_block, (((0,), (0,)), ((), ())), preferred_element_type=jnp.float32
        )
        grad_weight = grad_weight + part.astype(jnp.bfloat16).astype(jnp.float32)

    hidden_grad = lax.dot_general(
        all_back, weight_shard, (((1,), (1,)), ((), ())), preferred_element_type=jnp.float32
    )
    grad_gain = jnp.sum(hidden_grad * normed_cols, axis=0)

    partial_keys = jnp.dot(act_cols, weight_shard, preferred_element_type=jnp.float32)
    projected = lax.psum_scatter(partial_keys, "fsdp", scatter_dimension=0, tiled=True)
    my_cos = lax.dynamic_slice_in_dim(cosine, me * tok_rows, tok_rows, axis=0)
    my_sin = lax.dynamic_slice_in_dim(sine_part, me * tok_rows, tok_rows, axis=0)
    rotated = rotate(projected, my_cos, my_sin, 1.0).astype(jnp.bfloat16)
    return (
        rotated[None],
        grad_weight.astype(jnp.bfloat16)[None],
        grad_gain[None],
        new_outer,
        new_momentum,
    )


def _island_factors(n):
    if ISLAND_FACTORS is not None:
        return tuple(ISLAND_FACTORS)
    if n == 64:
        return (8, 4, 2)
    return (n,)


def solution(mesh):
    factors = _island_factors(mesh.shape["island"])
    island_axes = tuple(f"island{k}" for k in range(len(factors)))
    devices = np.asarray(mesh.devices).reshape(factors + (mesh.shape["fsdp"],))
    fine = Mesh(devices, island_axes + ("fsdp",))
    isl = island_axes
    placed = (
        P(isl, "fsdp", None),
        P("fsdp"),
        P(isl, "fsdp"),
        P(isl, "fsdp", None),
        P(isl, "fsdp", None),
        P(("fsdp",) + isl, None),
        P(("fsdp",) + isl, None),
    )
    return jax.shard_map(
        lambda *a: body(island_axes, *a),
        mesh=fine,
        in_specs=placed,
        out_specs=(
            P(isl, "fsdp", None),
            P(isl, "fsdp", None),
            P(isl, "fsdp"),
            P(("fsdp",) + isl, None),
            P(("fsdp",) + isl, None),
        ),
        check_vma=False,
    )
```

```python
import math

import jax
import jax.numpy as jnp
import numpy as np
from jax import lax
from jax.sharding import Mesh
from jax.sharding import PartitionSpec as P

HEAD = 128
DOCS = 8


learn_rate = 0.7
momentum_rate = 0.9
norm_eps = 1e-05
rope_base = 500000.0
far_index = 1 << 30

ISLAND_FACTORS = None


def angles_for(positions, head_width):
    half_width = head_width // 2
    frequency = jnp.exp(
        jnp.arange(half_width, dtype=jnp.float32) * (-2.0 * math.log(rope_base) / head_width)
    )
    phases = positions[:, None] * frequency[None, :]
    return (jnp.cos(phases), jnp.sin(phases))


def rotate(values, cosine, sine_part, sign):
    rows = values.shape[0]
    half_width = cosine.shape[1]
    shaped = values.reshape(rows, -1, 2 * half_width)
    leading = shaped[:, :, :half_width]
    second = shaped[:, :, half_width:]
    cos_b = cosine[:, None, :]
    sin_b = sine_part[:, None, :] * sign
    joined = jnp.concatenate(
        [leading * cos_b - second * sin_b, second * cos_b + leading * sin_b], axis=2
    )
    return joined.reshape(rows, -1)


def halving_scatter(values, axis):
    n = lax.axis_size(axis)
    me = lax.axis_index(axis)
    step = n // 2
    while step >= 1:
        rows = values.shape[0] // 2
        upper = (me // step) % 2
        keep = lax.dynamic_slice_in_dim(values, upper * rows, rows, axis=0)
        send = lax.dynamic_slice_in_dim(values, (1 - upper) * rows, rows, axis=0)
        got = lax.ppermute(send, axis, [(j, j ^ step) for j in range(n)])
        values = keep + got
        step //= 2
    return values


def doubling_gather(values, axis):
    n = lax.axis_size(axis)
    me = lax.axis_index(axis)
    step = 1
    while step < n:
        got = lax.ppermute(values, axis, [(j, j ^ step) for j in range(n)])
        upper = (me // step) % 2
        values = jnp.where(
            upper == 1,
            jnp.concatenate([got, values], axis=0),
            jnp.concatenate([values, got], axis=0),
        )
        step *= 2
    return values


def doubling_sum(values, axis):
    n = lax.axis_size(axis)
    step = 1 << (n.bit_length() - 2) if n > 1 else 0
    while step >= 1:
        values = values + lax.ppermute(values, axis, [(j, j ^ step) for j in range(n)])
        step //= 2
    return values


def body(island_axes, hidden, gain, doc_ids, cotangent, pseudo_grad, outer_weight, momentum):
    islands = 1
    for ax in island_axes:
        islands *= lax.axis_size(ax)
    fsdp_ways = lax.axis_size("fsdp")

    summed = pseudo_grad[0].astype(jnp.float32)
    summed = lax.psum_scatter(summed, island_axes[0], scatter_dimension=0, tiled=True)
    rest = island_axes[1:]
    state = jnp.concatenate([outer_weight, momentum], axis=1)
    for ax in reversed(rest):
        state = lax.all_gather(state, ax, axis=0, tiled=True)
    for ax in rest:
        summed = doubling_sum(summed, ax)
    cols = outer_weight.shape[1]
    group_outer, group_momentum = state[:, :cols], state[:, cols:]
    mean_delta = summed / islands
    group_new_momentum = momentum_rate * group_momentum + mean_delta
    group_new_outer = group_outer - learn_rate * (mean_delta + momentum_rate * group_new_momentum)
    weight_shard = group_new_outer.astype(jnp.bfloat16)
    weight_shard = lax.all_gather(weight_shard, island_axes[0], axis=0, tiled=True)
    mine = 0
    for ax in rest:
        mine = mine * lax.axis_size(ax) + lax.axis_index(ax)
    own_rows = outer_weight.shape[0]
    new_outer = lax.dynamic_slice_in_dim(group_new_outer, mine * own_rows, own_rows, axis=0)
    new_momentum = lax.dynamic_slice_in_dim(group_new_momentum, mine * own_rows, own_rows, axis=0)

    tok_rows = hidden.shape[1]
    seq = tok_rows * fsdp_ways
    me = lax.axis_index("fsdp")
    all_docs = lax.all_gather(doc_ids[0], "fsdp", axis=0, tiled=True)
    indices = jnp.arange(seq, dtype=jnp.int32)
    documents = jnp.arange(DOCS, dtype=jnp.int32)
    in_document = all_docs[:, None] == documents[None, :]
    starts = jnp.min(jnp.where(in_document, indices[:, None], far_index), axis=0)
    doc_start = jnp.sum(jnp.where(in_document, starts[None, :], 0), axis=1)
    positions = (indices - doc_start).astype(jnp.float32)
    cosine, sine_part = angles_for(positions, HEAD)
    width = hidden.shape[2] // fsdp_ways
    cols_out = cotangent.shape[2]
    outgoing = jnp.concatenate(
        [
            hidden[0].reshape(tok_rows, fsdp_ways, width).transpose(1, 0, 2),
            jnp.broadcast_to(cotangent[0][None], (fsdp_ways, tok_rows, cols_out)),
        ],
        axis=2,
    )
    incoming = lax.all_to_all(outgoing, "fsdp", split_axis=0, concat_axis=0, tiled=True)
    columns = incoming[:, :, :width].reshape(seq, width)
    all_cot = incoming[:, :, width:].reshape(seq, cols_out)
    all_back = rotate(all_cot.astype(jnp.float32), cosine, sine_part, -1.0).astype(jnp.bfloat16)

    hidden_f = hidden[0].astype(jnp.float32)
    row_scale = lax.rsqrt(jnp.mean(hidden_f * hidden_f, axis=1, keepdims=True) + norm_eps)
    all_scales = lax.all_gather(row_scale, "fsdp", axis=0, tiled=True)
    normed_cols = columns.astype(jnp.float32) * all_scales
    act_cols = (normed_cols * gain.astype(jnp.float32)[None, :]).astype(jnp.bfloat16)

    grad_weight = jnp.zeros((act_cols.shape[1], all_back.shape[1]), jnp.float32)
    for block in range(fsdp_ways):
        act_block = act_cols[block * tok_rows : (block + 1) * tok_rows]
        back_block = all_back[block * tok_rows : (block + 1) * tok_rows]
        part = lax.dot_general(
            act_block, back_block, (((0,), (0,)), ((), ())), preferred_element_type=jnp.float32
        )
        grad_weight = grad_weight + part.astype(jnp.bfloat16).astype(jnp.float32)

    hidden_grad = lax.dot_general(
        all_back, weight_shard, (((1,), (1,)), ((), ())), preferred_element_type=jnp.float32
    )
    grad_gain = jnp.sum(hidden_grad * normed_cols, axis=0)

    partial_keys = jnp.dot(act_cols, weight_shard, preferred_element_type=jnp.float32)
    projected = lax.psum_scatter(partial_keys, "fsdp", scatter_dimension=0, tiled=True)
    my_cos = lax.dynamic_slice_in_dim(cosine, me * tok_rows, tok_rows, axis=0)
    my_sin = lax.dynamic_slice_in_dim(sine_part, me * tok_rows, tok_rows, axis=0)
    rotated = rotate(projected, my_cos, my_sin, 1.0).astype(jnp.bfloat16)
    return (
        rotated[None],
        grad_weight.astype(jnp.bfloat16)[None],
        grad_gain[None],
        new_outer,
        new_momentum,
    )


def _island_factors(n):
    if ISLAND_FACTORS is not None:
        return tuple(ISLAND_FACTORS)
    if n == 64:
        return (8, 4, 2)
    return (n,)


def solution(mesh):
    factors = _island_factors(mesh.shape["island"])
    island_axes = tuple(f"island{k}" for k in range(len(factors)))
    devices = np.asarray(mesh.devices).reshape(factors + (mesh.shape["fsdp"],))
    fine = Mesh(devices, island_axes + ("fsdp",))
    isl = island_axes
    placed = (
        P(isl, "fsdp", None),
        P("fsdp"),
        P(isl, "fsdp"),
        P(isl, "fsdp", None),
        P(isl, "fsdp", None),
        P(("fsdp",) + isl, None),
        P(("fsdp",) + isl, None),
    )
    return jax.shard_map(
        lambda *a: body(island_axes, *a),
        mesh=fine,
        in_specs=placed,
        out_specs=(
            P(isl, "fsdp", None),
            P(isl, "fsdp", None),
            P(isl, "fsdp"),
            P(("fsdp",) + isl, None),
            P(("fsdp",) + isl, None),
        ),
        check_vma=False,
    )
```

```python
import math

import jax
import jax.numpy as jnp
import numpy as np
from jax import lax
from jax.sharding import Mesh
from jax.sharding import PartitionSpec as P

HEAD = 128
DOCS = 8


learn_rate = 0.7
momentum_rate = 0.9
norm_eps = 1e-05
rope_base = 500000.0
far_index = 1 << 30

ISLAND_FACTORS = None


def angles_for(positions, head_width):
    half_width = head_width // 2
    frequency = jnp.exp(
        jnp.arange(half_width, dtype=jnp.float32) * (-2.0 * math.log(rope_base) / head_width)
    )
    phases = positions[:, None] * frequency[None, :]
    return (jnp.cos(phases), jnp.sin(phases))


def rotate(values, cosine, sine_part, sign):
    rows = values.shape[0]
    half_width = cosine.shape[1]
    shaped = values.reshape(rows, -1, 2 * half_width)
    leading = shaped[:, :, :half_width]
    second = shaped[:, :, half_width:]
    cos_b = cosine[:, None, :]
    sin_b = sine_part[:, None, :] * sign
    joined = jnp.concatenate(
        [leading * cos_b - second * sin_b, second * cos_b + leading * sin_b], axis=2
    )
    return joined.reshape(rows, -1)


def halving_scatter(values, axis):
    n = lax.axis_size(axis)
    me = lax.axis_index(axis)
    step = n // 2
    while step >= 1:
        rows = values.shape[0] // 2
        upper = (me // step) % 2
        keep = lax.dynamic_slice_in_dim(values, upper * rows, rows, axis=0)
        send = lax.dynamic_slice_in_dim(values, (1 - upper) * rows, rows, axis=0)
        got = lax.ppermute(send, axis, [(j, j ^ step) for j in range(n)])
        values = keep + got
        step //= 2
    return values


def doubling_gather(values, axis):
    n = lax.axis_size(axis)
    me = lax.axis_index(axis)
    step = 1
    while step < n:
        got = lax.ppermute(values, axis, [(j, j ^ step) for j in range(n)])
        upper = (me // step) % 2
        values = jnp.where(
            upper == 1,
            jnp.concatenate([got, values], axis=0),
            jnp.concatenate([values, got], axis=0),
        )
        step *= 2
    return values


def doubling_sum(values, axis):
    n = lax.axis_size(axis)
    step = 1 << (n.bit_length() - 2) if n > 1 else 0
    while step >= 1:
        values = values + lax.ppermute(values, axis, [(j, j ^ step) for j in range(n)])
        step //= 2
    return values


def body(island_axes, hidden, gain, doc_ids, cotangent, pseudo_grad, outer_weight, momentum):
    islands = 1
    for ax in island_axes:
        islands *= lax.axis_size(ax)
    fsdp_ways = lax.axis_size("fsdp")

    summed = pseudo_grad[0].astype(jnp.float32)
    summed = lax.psum_scatter(summed, island_axes[0], scatter_dimension=0, tiled=True)
    rest = island_axes[1:]
    state = jnp.concatenate([outer_weight, momentum], axis=1)
    for ax in reversed(rest):
        state = doubling_gather(state, ax)
    for ax in rest:
        summed = doubling_sum(summed, ax)
    cols = outer_weight.shape[1]
    group_outer, group_momentum = state[:, :cols], state[:, cols:]
    mean_delta = summed / islands
    group_new_momentum = momentum_rate * group_momentum + mean_delta
    group_new_outer = group_outer - learn_rate * (mean_delta + momentum_rate * group_new_momentum)
    weight_shard = group_new_outer.astype(jnp.bfloat16)
    weight_shard = lax.all_gather(weight_shard, island_axes[0], axis=0, tiled=True)
    mine = 0
    for ax in rest:
        mine = mine * lax.axis_size(ax) + lax.axis_index(ax)
    own_rows = outer_weight.shape[0]
    new_outer = lax.dynamic_slice_in_dim(group_new_outer, mine * own_rows, own_rows, axis=0)
    new_momentum = lax.dynamic_slice_in_dim(group_new_momentum, mine * own_rows, own_rows, axis=0)

    tok_rows = hidden.shape[1]
    seq = tok_rows * fsdp_ways
    me = lax.axis_index("fsdp")
    all_docs = lax.all_gather(doc_ids[0], "fsdp", axis=0, tiled=True)
    indices = jnp.arange(seq, dtype=jnp.int32)
    documents = jnp.arange(DOCS, dtype=jnp.int32)
    in_document = all_docs[:, None] == documents[None, :]
    starts = jnp.min(jnp.where(in_document, indices[:, None], far_index), axis=0)
    doc_start = jnp.sum(jnp.where(in_document, starts[None, :], 0), axis=1)
    positions = (indices - doc_start).astype(jnp.float32)
    cosine, sine_part = angles_for(positions, HEAD)
    width = hidden.shape[2] // fsdp_ways
    cols_out = cotangent.shape[2]
    outgoing = jnp.concatenate(
        [
            hidden[0].reshape(tok_rows, fsdp_ways, width).transpose(1, 0, 2),
            jnp.broadcast_to(cotangent[0][None], (fsdp_ways, tok_rows, cols_out)),
        ],
        axis=2,
    )
    incoming = lax.all_to_all(outgoing, "fsdp", split_axis=0, concat_axis=0, tiled=True)
    columns = incoming[:, :, :width].reshape(seq, width)
    all_cot = incoming[:, :, width:].reshape(seq, cols_out)
    all_back = rotate(all_cot.astype(jnp.float32), cosine, sine_part, -1.0).astype(jnp.bfloat16)

    hidden_f = hidden[0].astype(jnp.float32)
    row_scale = lax.rsqrt(jnp.mean(hidden_f * hidden_f, axis=1, keepdims=True) + norm_eps)
    all_scales = lax.all_gather(row_scale, "fsdp", axis=0, tiled=True)
    normed_cols = columns.astype(jnp.float32) * all_scales
    act_cols = (normed_cols * gain.astype(jnp.float32)[None, :]).astype(jnp.bfloat16)

    grad_weight = jnp.zeros((act_cols.shape[1], all_back.shape[1]), jnp.float32)
    for block in range(fsdp_ways):
        act_block = act_cols[block * tok_rows : (block + 1) * tok_rows]
        back_block = all_back[block * tok_rows : (block + 1) * tok_rows]
        part = lax.dot_general(
            act_block, back_block, (((0,), (0,)), ((), ())), preferred_element_type=jnp.float32
        )
        grad_weight = grad_weight + part.astype(jnp.bfloat16).astype(jnp.float32)

    hidden_grad = lax.dot_general(
        all_back, weight_shard, (((1,), (1,)), ((), ())), preferred_element_type=jnp.float32
    )
    grad_gain = jnp.sum(hidden_grad * normed_cols, axis=0)

    partial_keys = jnp.dot(act_cols, weight_shard, preferred_element_type=jnp.float32)
    projected = lax.psum_scatter(partial_keys, "fsdp", scatter_dimension=0, tiled=True)
    my_cos = lax.dynamic_slice_in_dim(cosine, me * tok_rows, tok_rows, axis=0)
    my_sin = lax.dynamic_slice_in_dim(sine_part, me * tok_rows, tok_rows, axis=0)
    rotated = rotate(projected, my_cos, my_sin, 1.0).astype(jnp.bfloat16)
    return (
        rotated[None],
        grad_weight.astype(jnp.bfloat16)[None],
        grad_gain[None],
        new_outer,
        new_momentum,
    )


def _island_factors(n):
    if ISLAND_FACTORS is not None:
        return tuple(ISLAND_FACTORS)
    if n == 64:
        return (8, 4, 2)
    return (n,)


def solution(mesh):
    factors = _island_factors(mesh.shape["island"])
    island_axes = tuple(f"island{k}" for k in range(len(factors)))
    devices = np.asarray(mesh.devices).reshape(factors + (mesh.shape["fsdp"],))
    fine = Mesh(devices, island_axes + ("fsdp",))
    isl = island_axes
    placed = (
        P(isl, "fsdp", None),
        P("fsdp"),
        P(isl, "fsdp"),
        P(isl, "fsdp", None),
        P(isl, "fsdp", None),
        P(("fsdp",) + isl, None),
        P(("fsdp",) + isl, None),
    )
    return jax.shard_map(
        lambda *a: body(island_axes, *a),
        mesh=fine,
        in_specs=placed,
        out_specs=(
            P(isl, "fsdp", None),
            P(isl, "fsdp", None),
            P(isl, "fsdp"),
            P(("fsdp",) + isl, None),
            P(("fsdp",) + isl, None),
        ),
        check_vma=False,
    )
```

```python
import math

import jax
import jax.numpy as jnp
import numpy as np
from jax import lax
from jax.sharding import Mesh
from jax.sharding import PartitionSpec as P

HEAD = 128
DOCS = 8


learn_rate = 0.7
momentum_rate = 0.9
norm_eps = 1e-05
rope_base = 500000.0
far_index = 1 << 30

ISLAND_FACTORS = None


def angles_for(positions, head_width):
    half_width = head_width // 2
    frequency = jnp.exp(
        jnp.arange(half_width, dtype=jnp.float32) * (-2.0 * math.log(rope_base) / head_width)
    )
    phases = positions[:, None] * frequency[None, :]
    return (jnp.cos(phases), jnp.sin(phases))


def rotate(values, cosine, sine_part, sign):
    rows = values.shape[0]
    half_width = cosine.shape[1]
    shaped = values.reshape(rows, -1, 2 * half_width)
    leading = shaped[:, :, :half_width]
    second = shaped[:, :, half_width:]
    cos_b = cosine[:, None, :]
    sin_b = sine_part[:, None, :] * sign
    joined = jnp.concatenate(
        [leading * cos_b - second * sin_b, second * cos_b + leading * sin_b], axis=2
    )
    return joined.reshape(rows, -1)


def halving_scatter(values, axis):
    n = lax.axis_size(axis)
    me = lax.axis_index(axis)
    step = n // 2
    while step >= 1:
        rows = values.shape[0] // 2
        upper = (me // step) % 2
        keep = lax.dynamic_slice_in_dim(values, upper * rows, rows, axis=0)
        send = lax.dynamic_slice_in_dim(values, (1 - upper) * rows, rows, axis=0)
        got = lax.ppermute(send, axis, [(j, j ^ step) for j in range(n)])
        values = keep + got
        step //= 2
    return values


def doubling_gather(values, axis):
    n = lax.axis_size(axis)
    me = lax.axis_index(axis)
    step = 1
    while step < n:
        got = lax.ppermute(values, axis, [(j, j ^ step) for j in range(n)])
        upper = (me // step) % 2
        values = jnp.where(
            upper == 1,
            jnp.concatenate([got, values], axis=0),
            jnp.concatenate([values, got], axis=0),
        )
        step *= 2
    return values


def doubling_sum(values, axis):
    n = lax.axis_size(axis)
    step = 1 << (n.bit_length() - 2) if n > 1 else 0
    while step >= 1:
        values = values + lax.ppermute(values, axis, [(j, j ^ step) for j in range(n)])
        step //= 2
    return values


def body(island_axes, hidden, gain, doc_ids, cotangent, pseudo_grad, outer_weight, momentum):
    islands = 1
    for ax in island_axes:
        islands *= lax.axis_size(ax)
    fsdp_ways = lax.axis_size("fsdp")

    summed = pseudo_grad[0].astype(jnp.float32)
    summed = lax.psum_scatter(summed, island_axes[0], scatter_dimension=0, tiled=True)
    rest = island_axes[1:]
    state = jnp.concatenate([outer_weight, momentum], axis=1)
    first_gathered = None
    for ax in reversed(rest):
        state = doubling_gather(state, ax)
        if first_gathered is None:
            first_gathered = state
    for ax in rest:
        summed = doubling_sum(summed, ax)
    cols = outer_weight.shape[1]
    group_outer, group_momentum = state[:, :cols], state[:, cols:]
    mean_delta = summed / islands
    group_new_momentum = momentum_rate * group_momentum + mean_delta
    group_new_outer = group_outer - learn_rate * (mean_delta + momentum_rate * group_new_momentum)
    weight_shard = group_new_outer.astype(jnp.bfloat16)
    weight_shard = lax.all_gather(weight_shard, island_axes[0], axis=0, tiled=True)
    mine = 0
    for ax in rest:
        mine = mine * lax.axis_size(ax) + lax.axis_index(ax)
    own_rows = outer_weight.shape[0]
    new_outer = lax.dynamic_slice_in_dim(group_new_outer, mine * own_rows, own_rows, axis=0)
    new_momentum = lax.dynamic_slice_in_dim(group_new_momentum, mine * own_rows, own_rows, axis=0)

    tok_rows = hidden.shape[1]
    seq = tok_rows * fsdp_ways
    me = lax.axis_index("fsdp")
    all_docs = lax.all_gather(doc_ids[0], "fsdp", axis=0, tiled=True)
    indices = jnp.arange(seq, dtype=jnp.int32)
    documents = jnp.arange(DOCS, dtype=jnp.int32)
    in_document = all_docs[:, None] == documents[None, :]
    starts = jnp.min(jnp.where(in_document, indices[:, None], far_index), axis=0)
    doc_start = jnp.sum(jnp.where(in_document, starts[None, :], 0), axis=1)
    positions = (indices - doc_start).astype(jnp.float32)
    cosine, sine_part = angles_for(positions, HEAD)
    width = hidden.shape[2] // fsdp_ways
    cols_out = cotangent.shape[2]
    outgoing = jnp.concatenate(
        [
            hidden[0].reshape(tok_rows, fsdp_ways, width).transpose(1, 0, 2),
            jnp.broadcast_to(cotangent[0][None], (fsdp_ways, tok_rows, cols_out)),
        ],
        axis=2,
    )
    if first_gathered is not None:
        _, outgoing = lax.optimization_barrier((first_gathered, outgoing))
    incoming = lax.all_to_all(outgoing, "fsdp", split_axis=0, concat_axis=0, tiled=True)
    columns = incoming[:, :, :width].reshape(seq, width)
    all_cot = incoming[:, :, width:].reshape(seq, cols_out)
    all_back = rotate(all_cot.astype(jnp.float32), cosine, sine_part, -1.0).astype(jnp.bfloat16)

    hidden_f = hidden[0].astype(jnp.float32)
    row_scale = lax.rsqrt(jnp.mean(hidden_f * hidden_f, axis=1, keepdims=True) + norm_eps)
    all_scales = lax.all_gather(row_scale, "fsdp", axis=0, tiled=True)
    normed_cols = columns.astype(jnp.float32) * all_scales
    act_cols = (normed_cols * gain.astype(jnp.float32)[None, :]).astype(jnp.bfloat16)

    grad_weight = jnp.zeros((act_cols.shape[1], all_back.shape[1]), jnp.float32)
    for block in range(fsdp_ways):
        act_block = act_cols[block * tok_rows : (block + 1) * tok_rows]
        back_block = all_back[block * tok_rows : (block + 1) * tok_rows]
        part = lax.dot_general(
            act_block, back_block, (((0,), (0,)), ((), ())), preferred_element_type=jnp.float32
        )
        grad_weight = grad_weight + part.astype(jnp.bfloat16).astype(jnp.float32)

    hidden_grad = lax.dot_general(
        all_back, weight_shard, (((1,), (1,)), ((), ())), preferred_element_type=jnp.float32
    )
    grad_gain = jnp.sum(hidden_grad * normed_cols, axis=0)

    partial_keys = jnp.dot(act_cols, weight_shard, preferred_element_type=jnp.float32)
    projected = lax.psum_scatter(partial_keys, "fsdp", scatter_dimension=0, tiled=True)
    my_cos = lax.dynamic_slice_in_dim(cosine, me * tok_rows, tok_rows, axis=0)
    my_sin = lax.dynamic_slice_in_dim(sine_part, me * tok_rows, tok_rows, axis=0)
    rotated = rotate(projected, my_cos, my_sin, 1.0).astype(jnp.bfloat16)
    return (
        rotated[None],
        grad_weight.astype(jnp.bfloat16)[None],
        grad_gain[None],
        new_outer,
        new_momentum,
    )


def _island_factors(n):
    if ISLAND_FACTORS is not None:
        return tuple(ISLAND_FACTORS)
    if n == 64:
        return (8, 4, 2)
    return (n,)


def solution(mesh):
    factors = _island_factors(mesh.shape["island"])
    island_axes = tuple(f"island{k}" for k in range(len(factors)))
    devices = np.asarray(mesh.devices).reshape(factors + (mesh.shape["fsdp"],))
    fine = Mesh(devices, island_axes + ("fsdp",))
    isl = island_axes
    placed = (
        P(isl, "fsdp", None),
        P("fsdp"),
        P(isl, "fsdp"),
        P(isl, "fsdp", None),
        P(isl, "fsdp", None),
        P(("fsdp",) + isl, None),
        P(("fsdp",) + isl, None),
    )
    return jax.shard_map(
        lambda *a: body(island_axes, *a),
        mesh=fine,
        in_specs=placed,
        out_specs=(
            P(isl, "fsdp", None),
            P(isl, "fsdp", None),
            P(isl, "fsdp"),
            P(("fsdp",) + isl, None),
            P(("fsdp",) + isl, None),
        ),
        check_vma=False,
    )
```

```python
import math

import jax
import jax.numpy as jnp
import numpy as np
from jax import lax
from jax.sharding import Mesh
from jax.sharding import PartitionSpec as P

HEAD = 128
DOCS = 8


learn_rate = 0.7
momentum_rate = 0.9
norm_eps = 1e-05
rope_base = 500000.0
far_index = 1 << 30

ISLAND_FACTORS = None


def angles_for(positions, head_width):
    half_width = head_width // 2
    frequency = jnp.exp(
        jnp.arange(half_width, dtype=jnp.float32) * (-2.0 * math.log(rope_base) / head_width)
    )
    phases = positions[:, None] * frequency[None, :]
    return (jnp.cos(phases), jnp.sin(phases))


def rotate(values, cosine, sine_part, sign):
    rows = values.shape[0]
    half_width = cosine.shape[1]
    shaped = values.reshape(rows, -1, 2 * half_width)
    leading = shaped[:, :, :half_width]
    second = shaped[:, :, half_width:]
    cos_b = cosine[:, None, :]
    sin_b = sine_part[:, None, :] * sign
    joined = jnp.concatenate(
        [leading * cos_b - second * sin_b, second * cos_b + leading * sin_b], axis=2
    )
    return joined.reshape(rows, -1)


def halving_scatter(values, axis):
    n = lax.axis_size(axis)
    me = lax.axis_index(axis)
    step = n // 2
    while step >= 1:
        rows = values.shape[0] // 2
        upper = (me // step) % 2
        keep = lax.dynamic_slice_in_dim(values, upper * rows, rows, axis=0)
        send = lax.dynamic_slice_in_dim(values, (1 - upper) * rows, rows, axis=0)
        got = lax.ppermute(send, axis, [(j, j ^ step) for j in range(n)])
        values = keep + got
        step //= 2
    return values


def doubling_gather(values, axis):
    n = lax.axis_size(axis)
    me = lax.axis_index(axis)
    step = 1
    while step < n:
        got = lax.ppermute(values, axis, [(j, j ^ step) for j in range(n)])
        upper = (me // step) % 2
        values = jnp.where(
            upper == 1,
            jnp.concatenate([got, values], axis=0),
            jnp.concatenate([values, got], axis=0),
        )
        step *= 2
    return values


def doubling_sum(values, axis):
    n = lax.axis_size(axis)
    step = 1 << (n.bit_length() - 2) if n > 1 else 0
    while step >= 1:
        values = values + lax.ppermute(values, axis, [(j, j ^ step) for j in range(n)])
        step //= 2
    return values


def body(island_axes, hidden, gain, doc_ids, cotangent, pseudo_grad, outer_weight, momentum):
    islands = 1
    for ax in island_axes:
        islands *= lax.axis_size(ax)
    fsdp_ways = lax.axis_size("fsdp")

    summed = pseudo_grad[0].astype(jnp.float32)
    summed = lax.psum_scatter(summed, island_axes[0], scatter_dimension=0, tiled=True)
    rest = island_axes[1:]
    state = jnp.concatenate([outer_weight, momentum], axis=1)
    first_gathered = None
    for ax in reversed(rest):
        state = doubling_gather(state, ax)
        if first_gathered is None:
            first_gathered = state
    for ax in rest:
        summed = doubling_sum(summed, ax)
    cols = outer_weight.shape[1]
    group_outer, group_momentum = state[:, :cols], state[:, cols:]
    mean_delta = summed / islands
    group_new_momentum = momentum_rate * group_momentum + mean_delta
    group_new_outer = group_outer - learn_rate * (mean_delta + momentum_rate * group_new_momentum)
    weight_shard = group_new_outer.astype(jnp.bfloat16)
    weight_shard = lax.all_gather(weight_shard, island_axes[0], axis=0, tiled=True)
    mine = 0
    for ax in rest:
        mine = mine * lax.axis_size(ax) + lax.axis_index(ax)
    own_rows = outer_weight.shape[0]
    new_outer = lax.dynamic_slice_in_dim(group_new_outer, mine * own_rows, own_rows, axis=0)
    new_momentum = lax.dynamic_slice_in_dim(group_new_momentum, mine * own_rows, own_rows, axis=0)

    tok_rows = hidden.shape[1]
    seq = tok_rows * fsdp_ways
    me = lax.axis_index("fsdp")
    indices = jnp.arange(seq, dtype=jnp.int32)
    documents = jnp.arange(DOCS, dtype=jnp.int32)
    hidden_f = hidden[0].astype(jnp.float32)
    row_scale = lax.rsqrt(jnp.mean(hidden_f * hidden_f, axis=1, keepdims=True) + norm_eps)
    width = hidden.shape[2] // fsdp_ways
    cols_out = cotangent.shape[2]
    scale_high = lax.reduce_precision(row_scale, exponent_bits=8, mantissa_bits=7)
    scale_mid = lax.reduce_precision(row_scale - scale_high, exponent_bits=8, mantissa_bits=7)
    scale_low = row_scale - scale_high - scale_mid
    extras = jnp.concatenate(
        [doc_ids[0][:, None].astype(jnp.float32), scale_high, scale_mid, scale_low], axis=1
    ).astype(jnp.bfloat16)
    extras = jnp.pad(extras, ((0, 0), (0, 128 - extras.shape[1])))
    outgoing = jnp.concatenate(
        [
            hidden[0].reshape(tok_rows, fsdp_ways, width).transpose(1, 0, 2),
            jnp.broadcast_to(cotangent[0][None], (fsdp_ways, tok_rows, cols_out)),
            jnp.broadcast_to(extras[None], (fsdp_ways,) + extras.shape),
        ],
        axis=2,
    )
    if first_gathered is not None:
        _, outgoing = lax.optimization_barrier((first_gathered, outgoing))
    incoming = lax.all_to_all(outgoing, "fsdp", split_axis=0, concat_axis=0, tiled=True)
    columns = incoming[:, :, :width].reshape(seq, width)
    all_cot = incoming[:, :, width : width + cols_out].reshape(seq, cols_out)
    all_extras = incoming[:, :, width + cols_out :].reshape(seq, -1).astype(jnp.float32)
    all_docs = all_extras[:, 0].astype(jnp.int32)
    all_scales = (all_extras[:, 1:2] + all_extras[:, 2:3]) + all_extras[:, 3:4]
    in_document = all_docs[:, None] == documents[None, :]
    starts = jnp.min(jnp.where(in_document, indices[:, None], far_index), axis=0)
    doc_start = jnp.sum(jnp.where(in_document, starts[None, :], 0), axis=1)
    positions = (indices - doc_start).astype(jnp.float32)
    cosine, sine_part = angles_for(positions, HEAD)
    all_back = rotate(all_cot.astype(jnp.float32), cosine, sine_part, -1.0).astype(jnp.bfloat16)

    normed_cols = columns.astype(jnp.float32) * all_scales
    act_cols = (normed_cols * gain.astype(jnp.float32)[None, :]).astype(jnp.bfloat16)

    grad_weight = jnp.zeros((act_cols.shape[1], all_back.shape[1]), jnp.float32)
    for block in range(fsdp_ways):
        act_block = act_cols[block * tok_rows : (block + 1) * tok_rows]
        back_block = all_back[block * tok_rows : (block + 1) * tok_rows]
        part = lax.dot_general(
            act_block, back_block, (((0,), (0,)), ((), ())), preferred_element_type=jnp.float32
        )
        grad_weight = grad_weight + part.astype(jnp.bfloat16).astype(jnp.float32)

    hidden_grad = lax.dot_general(
        all_back, weight_shard, (((1,), (1,)), ((), ())), preferred_element_type=jnp.float32
    )
    grad_gain = jnp.sum(hidden_grad * normed_cols, axis=0)

    partial_keys = jnp.dot(act_cols, weight_shard, preferred_element_type=jnp.float32)
    projected = lax.psum_scatter(partial_keys, "fsdp", scatter_dimension=0, tiled=True)
    my_cos = lax.dynamic_slice_in_dim(cosine, me * tok_rows, tok_rows, axis=0)
    my_sin = lax.dynamic_slice_in_dim(sine_part, me * tok_rows, tok_rows, axis=0)
    rotated = rotate(projected, my_cos, my_sin, 1.0).astype(jnp.bfloat16)
    return (
        rotated[None],
        grad_weight.astype(jnp.bfloat16)[None],
        grad_gain[None],
        new_outer,
        new_momentum,
    )


def _island_factors(n):
    if ISLAND_FACTORS is not None:
        return tuple(ISLAND_FACTORS)
    if n == 64:
        return (8, 4, 2)
    return (n,)


def solution(mesh):
    factors = _island_factors(mesh.shape["island"])
    island_axes = tuple(f"island{k}" for k in range(len(factors)))
    devices = np.asarray(mesh.devices).reshape(factors + (mesh.shape["fsdp"],))
    fine = Mesh(devices, island_axes + ("fsdp",))
    isl = island_axes
    placed = (
        P(isl, "fsdp", None),
        P("fsdp"),
        P(isl, "fsdp"),
        P(isl, "fsdp", None),
        P(isl, "fsdp", None),
        P(("fsdp",) + isl, None),
        P(("fsdp",) + isl, None),
    )
    return jax.shard_map(
        lambda *a: body(island_axes, *a),
        mesh=fine,
        in_specs=placed,
        out_specs=(
            P(isl, "fsdp", None),
            P(isl, "fsdp", None),
            P(isl, "fsdp"),
            P(("fsdp",) + isl, None),
            P(("fsdp",) + isl, None),
        ),
        check_vma=False,
    )
```
